256 devices in a mesh: gene: 4 (over z_lo, core), cell: 16 (over z_hi, y), site: 4 (over x).
Axes of the slice: x: 4, y: 4, z: 8 (z_hi: 4, z_lo: 2; z = z_hi * 2 + z_lo), core: 2. Of those that a mesh axis runs over, the one named last changes fastest.
Arguments:
- expr: bfloat16 [8192, 20000], P('cell', 'gene'), may hold values from -6 to 6
- proj_weight: bfloat16 [20000, 512], P('gene'), may hold values from -0.0390625 to 0.0390625
- centroids: bfloat16 [8192, 512], P('site'), may hold values from -6 to 6
- growth: float32 [8192], P('cell'), may hold values from 0.5 to 6
- site_weight: float32 [8192], P('site'), may hold values from 0.5 to 6
Outputs:
- cell_pot: float32 [8192], P('cell')
- site_pot: float32 [8192], P('site')
- barycenter: float32 [8192, 512], P('site')
The draws below stay inside these ranges and needn't reach their ends.
All inputs are finite; a program needn't handle non-finite values.
Results may differ from the reference program's by a relative error of at most 0.0033.
The reference program's roundings to bfloat16 on the way (of `projected` and `coupling`) count: a program that leaves them out, or rounds other values in their place, can miss the bound.
Values may be sent and summed in bfloat16 or wider, within the bound.
No kernel may reach another device: no remote copies, remote signals or barrier semaphores. Data moves between devices by JAX's collectives and lax.ppermute only.
A program may use at most 64 MiB of HBM per device.

```python
import math
import jax
import jax.numpy as jnp
from jax import lax

G = 20000
K = 512
ROUNDS = 2
CELLS = 8192
SITES = 8192


def ramped(key, length):
    base = jnp.exp(jax.random.uniform(key, (length,), jnp.float32, math.log(0.5), math.log(2.0)))
    ramp = 1.0 + 2.0 * jnp.arange(length).astype(jnp.float32) / max(length - 1, 1)
    return base * ramp


def draw_growth(key, part):
    return ramped(jax.random.fold_in(key, 11), CELLS)


def draw_site_weight(key, part):
    return ramped(jax.random.fold_in(key, 23), SITES)


def levels(rng, extent, pieces, least, largest):
    level = 1.0
    for axis_at, parts in pieces:
        draws = jax.random.uniform(jax.random.fold_in(jax.random.fold_in(rng, 6), axis_at), (parts,), jnp.float32, least / len(pieces), largest / len(pieces))
        level = level * jnp.repeat(jnp.exp(draws), extent[axis_at] // parts).reshape((-1,) + (1,) * (len(extent) - 1 - axis_at))
    return level


def normal_values(own_key, shape, scale, reach, split=(), dtype=jnp.bfloat16):
    entries = jax.random.normal(own_key, shape, jnp.float32) * scale
    if len(split) > 0:
        entries = levels(own_key, shape, split, -0.22, 0.18) * entries
    return jnp.clip(entries, min=-reach, max=reach).astype(dtype)


def setup_inputs(seed: int = 0) -> dict:
    keys = jax.random.split(jax.random.key(seed), 6)
    return {
        "expr": normal_values(keys[0], (CELLS, G), 1.0, 6.0, ((0, 16), (1, 4))),
        "proj_weight": normal_values(keys[1], (G, K), G ** -0.5, 0.0390625, ((0, 4),)),
        "centroids": normal_values(keys[2], (SITES, K), 1.0, 6.0, ((0, 4),)),
        "growth": draw_growth(jax.random.fold_in(keys[5], 71), 0),
        "site_weight": draw_site_weight(jax.random.fold_in(keys[5], 71), 0),
    }


EPSILON = 0.02


def log_sum_exp(scores, axis_index):
    peak = jnp.max(scores, axis=axis_index, keepdims=True)
    summed = jnp.sum(jnp.exp(scores - peak), axis=axis_index)
    return jnp.squeeze(peak, axis_index) + jnp.log(summed)


def reference(expr, proj_weight, centroids, growth, site_weight):
    projected = jnp.dot(expr, proj_weight, preferred_element_type=jnp.float32).astype(jnp.bfloat16)
    proj_f = projected.astype(jnp.float32)
    cent_f = centroids.astype(jnp.float32)
    proj_norm = jnp.sum(proj_f * proj_f, axis=1) / K
    cent_norm = jnp.sum(cent_f * cent_f, axis=1) / K
    cross = lax.dot_general(projected, centroids, (((1,), (1,)), ((), ())), preferred_element_type=jnp.float32)
    distance = proj_norm[:, None] + cent_norm[None, :] - 2.0 * cross / K
    log_a = jnp.log(growth / jnp.sum(growth))
    site_share = site_weight / jnp.sum(site_weight)
    log_b = jnp.log(site_share)
    site_pot = jnp.zeros((SITES,), jnp.float32)
    cell_pot = jnp.zeros((CELLS,), jnp.float32)
    for turn in range(ROUNDS):
        cell_pot = EPSILON * log_a - EPSILON * log_sum_exp((site_pot[None, :] - distance) / EPSILON, 1)
        site_pot = EPSILON * log_b - EPSILON * log_sum_exp((cell_pot[:, None] - distance) / EPSILON, 0)
    coupling = jnp.exp((cell_pot[:, None] + site_pot[None, :] - distance) / EPSILON).astype(jnp.bfloat16)
    carried = lax.dot_general(coupling, projected, (((0,), (0,)), ((), ())), preferred_element_type=jnp.float32)
    barycenter = carried / site_share[:, None]
    return (cell_pot, site_pot, barycenter)
```

```python
import jax
import jax.numpy as jnp
from jax import lax
from jax.sharding import Mesh
from jax.sharding import PartitionSpec as P

ROUNDS = 2
GENE = ("gene_0", "gene_1")
GENE_SITE = ("gene_0", "gene_1", "site")
GENE_CELL = ("gene_0", "gene_1", "cell")


EPSILON = 0.02


def lse_over(local_peak, local_sum, axis):
    both = lax.all_gather(jnp.stack([local_peak, local_sum]), axis, axis=0)
    peaks, sums = both[:, 0], both[:, 1]
    peak = jnp.max(peaks, axis=0)
    summed = jnp.sum(sums * jnp.exp(peaks - peak[None]), axis=0)
    return peak + jnp.log(summed)


def over_sites(scores):
    local_peak = jnp.max(scores, axis=1)
    local_sum = jnp.sum(jnp.exp(scores - local_peak[:, None]), axis=1)
    return lse_over(local_peak, local_sum, "site")


def over_cells(scores):
    local_peak = jnp.max(scores, axis=0)
    local_sum = jnp.sum(jnp.exp(scores - local_peak[None, :]), axis=0)
    return lse_over(local_peak, local_sum, "cell")


def shards(expr, proj_weight, centroids, growth, site_weight):
    cell_rows = expr.shape[0]
    site_rows = centroids.shape[0]
    features = proj_weight.shape[1]
    gene_count = lax.axis_size(GENE)
    site_count = lax.axis_size("site")
    cell_count = lax.axis_size("cell")
    block_rows = cell_rows // (gene_count * site_count)
    partial = jnp.dot(expr, proj_weight, preferred_element_type=jnp.float32)
    grouped = partial.reshape(gene_count, site_count, block_rows, features)
    own_rows = lax.dynamic_index_in_dim(grouped, lax.axis_index("site"), 1, keepdims=False)
    own_rows = own_rows.reshape(gene_count * block_rows, features)
    row_share = lax.psum_scatter(own_rows, GENE, scatter_dimension=0, tiled=True)
    projected = lax.all_gather(row_share.astype(jnp.bfloat16), GENE_SITE, axis=0, tiled=True)
    proj_f = projected.astype(jnp.float32)
    cent_f = centroids.astype(jnp.float32)
    proj_norm = jnp.sum(proj_f * proj_f, axis=1) / features
    cent_norm = jnp.sum(cent_f * cent_f, axis=1) / features
    cross = lax.dot_general(
        projected, centroids, (((1,), (1,)), ((), ())), preferred_element_type=jnp.float32
    )
    distance = proj_norm[:, None] + cent_norm[None, :] - 2.0 * cross / features
    growth_total = lax.psum(jnp.sum(growth), "cell")
    weight_total = lax.psum(jnp.sum(site_weight), "site")
    log_a = jnp.log(growth / growth_total)
    site_share = site_weight / weight_total
    log_b = jnp.log(site_share)
    site_pot = jnp.zeros((site_rows,), jnp.float32)
    cell_pot = jnp.zeros((cell_rows,), jnp.float32)
    for turn in range(ROUNDS):
        cell_pot = EPSILON * log_a - EPSILON * over_sites((site_pot[None, :] - distance) / EPSILON)
        site_pot = EPSILON * log_b - EPSILON * over_cells((cell_pot[:, None] - distance) / EPSILON)
    coupling = jnp.exp((cell_pot[:, None] + site_pot[None, :] - distance) / EPSILON).astype(
        jnp.bfloat16
    )
    gene_sites = site_rows // gene_count
    gene_at = lax.axis_index(GENE)
    site_part = lax.dynamic_slice_in_dim(coupling, gene_at * gene_sites, gene_sites, 1)
    carried = lax.dot_general(
        site_part, projected, (((0,), (0,)), ((), ())), preferred_element_type=jnp.float32
    )
    piece = lax.psum_scatter(carried, "cell", scatter_dimension=0, tiled=True)
    piece_rows = gene_sites // cell_count
    piece_at = gene_at * gene_sites + lax.axis_index("cell") * piece_rows
    share_part = lax.dynamic_slice_in_dim(site_share, piece_at, piece_rows, 0)
    scaled = piece / share_part[:, None]
    barycenter = lax.all_gather(scaled, GENE_CELL, axis=0, tiled=True)
    return (cell_pot, site_pot, barycenter)


def solution(mesh):
    torus = Mesh(
        mesh.devices.reshape(2, 2, mesh.shape["cell"], mesh.shape["site"]),
        ("gene_0", "gene_1", "cell", "site"),
    )
    return jax.shard_map(
        shards,
        mesh=torus,
        in_specs=(P("cell", GENE), P(GENE, None), P("site", None), P("cell"), P("site")),
        out_specs=(P("cell"), P("site"), P("site", None)),
        check_vma=False,
    )
```

```python
import jax
import jax.numpy as jnp
from jax import lax
from jax.sharding import Mesh
from jax.sharding import PartitionSpec as P

ROUNDS = 2
GENE = ("gene_0", "gene_1")
GENE_SITE = ("gene_0", "gene_1", "site")


EPSILON = 0.02


def from_everyone(x, axis):
    length = lax.axis_size(axis)
    return lax.all_to_all(jnp.broadcast_to(x[None], (length, *x.shape)), axis, 0, 0, tiled=True)


def split_up(x, dim, length):
    shape = x.shape
    tiles = x.reshape(*shape[:dim], length, shape[dim] // length, *shape[dim + 1 :])
    return jnp.moveaxis(tiles, dim, 0)


def summed_on_arrival(x, axis, dim):
    length = lax.axis_size(axis)
    tiles = lax.all_to_all(split_up(x, dim, length), axis, 0, 0, tiled=True)
    return jnp.sum(tiles, axis=0)


def gathered_rows(x, axis):
    tiles = from_everyone(x, axis)
    return tiles.reshape(tiles.shape[0] * tiles.shape[1], *tiles.shape[2:])


def lse_with_total(local_peak, local_sum, partial, axis):
    width = local_peak.shape[0]
    line = jnp.concatenate([local_peak, local_sum, jnp.broadcast_to(partial, (128,))])
    both = from_everyone(line, axis)
    peaks, sums = both[:, :width], both[:, width : 2 * width]
    total = jnp.sum(both[:, 2 * width])
    peak = jnp.max(peaks, axis=0)
    summed = jnp.sum(sums * jnp.exp(peaks - peak[None]), axis=0)
    return peak + jnp.log(summed), total


def over_sites(scores, partial):
    local_peak = jnp.max(scores, axis=1)
    local_sum = jnp.sum(jnp.exp(scores - local_peak[:, None]), axis=1)
    return lse_with_total(local_peak, local_sum, partial, "site")


def over_cells(scores, partial):
    local_peak = jnp.max(scores, axis=0)
    local_sum = jnp.sum(jnp.exp(scores - local_peak[None, :]), axis=0)
    return lse_with_total(local_peak, local_sum, partial, "cell")


def shards(expr, proj_weight, centroids, growth, site_weight):
    cell_rows = expr.shape[0]
    site_rows = centroids.shape[0]
    features = proj_weight.shape[1]
    gene_count = lax.axis_size(GENE)
    site_count = lax.axis_size("site")
    block_rows = cell_rows // (gene_count * site_count)
    partial = jnp.dot(expr, proj_weight, preferred_element_type=jnp.float32)
    grouped = partial.reshape(gene_count, site_count, block_rows, features)
    own_rows = lax.dynamic_index_in_dim(grouped, lax.axis_index("site"), 1, keepdims=False)
    own_rows = own_rows.reshape(gene_count * block_rows, features)
    row_share = summed_on_arrival(own_rows, GENE, 0)
    projected = gathered_rows(row_share.astype(jnp.bfloat16), GENE_SITE)
    proj_f = projected.astype(jnp.float32)
    cent_f = centroids.astype(jnp.float32)
    proj_norm = jnp.sum(proj_f * proj_f, axis=1) / features
    cent_norm = jnp.sum(cent_f * cent_f, axis=1) / features
    cross = lax.dot_general(
        projected, centroids, (((1,), (1,)), ((), ())), preferred_element_type=jnp.float32
    )
    distance = proj_norm[:, None] + cent_norm[None, :] - 2.0 * cross / features
    site_pot = jnp.zeros((site_rows,), jnp.float32)
    first_lse, weight_total = over_sites((site_pot[None, :] - distance) / EPSILON, jnp.sum(site_weight))
    site_share = site_weight / weight_total
    log_b = jnp.log(site_share)
    shifted = EPSILON * jnp.log(growth) - EPSILON * first_lse
    shifted_lse, growth_total = over_cells((shifted[:, None] - distance) / EPSILON, jnp.sum(growth))
    log_a = jnp.log(growth / growth_total)
    cell_pot = EPSILON * log_a - EPSILON * first_lse
    site_pot = EPSILON * log_b - EPSILON * (shifted_lse - jnp.log(growth_total))
    for turn in range(1, ROUNDS):
        lse, _ = over_sites((site_pot[None, :] - distance) / EPSILON, 0.0)
        cell_pot = EPSILON * log_a - EPSILON * lse
        lse, _ = over_cells((cell_pot[:, None] - distance) / EPSILON, 0.0)
        site_pot = EPSILON * log_b - EPSILON * lse
    gene_sites = site_rows // gene_count
    site_from = lax.axis_index(GENE) * gene_sites
    part_distance = lax.dynamic_slice_in_dim(distance, site_from, gene_sites, 1)
    part_pot = lax.dynamic_slice_in_dim(site_pot, site_from, gene_sites, 0)
    coupling = jnp.exp((cell_pot[:, None] + part_pot[None, :] - part_distance) / EPSILON).astype(
        jnp.bfloat16
    )
    carried = lax.dot_general(
        coupling, projected, (((0,), (0,)), ((), ())), preferred_element_type=jnp.float32
    )
    piece = summed_on_arrival(carried, "cell", 0)
    piece_rows = piece.shape[0]
    piece_at = site_from + lax.axis_index("cell") * piece_rows
    share_part = lax.dynamic_slice_in_dim(site_share, piece_at, piece_rows, 0)
    scaled = piece / share_part[:, None]
    barycenter = gathered_rows(gathered_rows(scaled, "cell"), GENE)
    return (cell_pot, site_pot, barycenter)


def solution(mesh):
    torus = Mesh(
        mesh.devices.reshape(2, 2, mesh.shape["cell"], mesh.shape["site"]),
        ("gene_0", "gene_1", "cell", "site"),
    )
    return jax.shard_map(
        shards,
        mesh=torus,
        in_specs=(P("cell", GENE), P(GENE, None), P("site", None), P("cell"), P("site")),
        out_specs=(P("cell"), P("site"), P("site", None)),
        check_vma=False,
    )
```

```python
import jax
import jax.numpy as jnp
from jax import lax
from jax.sharding import Mesh
from jax.sharding import PartitionSpec as P

ROUNDS = 2
GENE = ("gene_0", "gene_1")
GENE_SITE = ("gene_0", "gene_1", "site")
PLANE = ("gene_0", "cell")


EPSILON = 0.02


def from_everyone(x, axis):
    length = lax.axis_size(axis)
    return lax.all_to_all(jnp.broadcast_to(x[None], (length, *x.shape)), axis, 0, 0, tiled=True)


def split_up(x, dim, length):
    shape = x.shape
    tiles = x.reshape(*shape[:dim], length, shape[dim] // length, *shape[dim + 1 :])
    return jnp.moveaxis(tiles, dim, 0)


def summed_on_arrival(x, axis, dim):
    length = lax.axis_size(axis)
    tiles = lax.all_to_all(split_up(x, dim, length), axis, 0, 0, tiled=True)
    return jnp.sum(tiles, axis=0)


def gathered_rows(x, axis):
    tiles = from_everyone(x, axis)
    return tiles.reshape(tiles.shape[0] * tiles.shape[1], *tiles.shape[2:])


def lse_with_total(local_peak, local_sum, partial, axis):
    width = local_peak.shape[0]
    line = jnp.concatenate([local_peak, local_sum, jnp.broadcast_to(partial, (128,))])
    both = from_everyone(line, axis)
    peaks, sums = both[:, :width], both[:, width : 2 * width]
    total = jnp.sum(both[:, 2 * width])
    peak = jnp.max(peaks, axis=0)
    summed = jnp.sum(sums * jnp.exp(peaks - peak[None]), axis=0)
    return peak + jnp.log(summed), total


def over_sites(scores, partial):
    local_peak = jnp.max(scores, axis=1)
    local_sum = jnp.sum(jnp.exp(scores - local_peak[:, None]), axis=1)
    return lse_with_total(local_peak, local_sum, partial, "site")


def over_cells(scores, partial):
    local_peak = jnp.max(scores, axis=0)
    local_sum = jnp.sum(jnp.exp(scores - local_peak[None, :]), axis=0)
    return lse_with_total(local_peak, local_sum, partial, "cell")


def shards(expr, proj_weight, centroids, growth, site_weight):
    cell_rows = expr.shape[0]
    site_rows = centroids.shape[0]
    features = proj_weight.shape[1]
    gene_count = lax.axis_size(GENE)
    site_count = lax.axis_size("site")
    block_rows = cell_rows // (gene_count * site_count)
    partial = jnp.dot(expr, proj_weight, preferred_element_type=jnp.float32)
    grouped = partial.reshape(gene_count, site_count, block_rows, features)
    own_rows = lax.dynamic_index_in_dim(grouped, lax.axis_index("site"), 1, keepdims=False)
    own_rows = own_rows.reshape(gene_count * block_rows, features)
    row_share = summed_on_arrival(own_rows, GENE, 0)
    projected = gathered_rows(row_share.astype(jnp.bfloat16), GENE_SITE)
    proj_f = projected.astype(jnp.float32)
    cent_f = centroids.astype(jnp.float32)
    proj_norm = jnp.sum(proj_f * proj_f, axis=1) / features
    cent_norm = jnp.sum(cent_f * cent_f, axis=1) / features
    cross = lax.dot_general(
        projected, centroids, (((1,), (1,)), ((), ())), preferred_element_type=jnp.float32
    )
    distance = proj_norm[:, None] + cent_norm[None, :] - 2.0 * cross / features
    site_pot = jnp.zeros((site_rows,), jnp.float32)
    first_lse, weight_total = over_sites((site_pot[None, :] - distance) / EPSILON, jnp.sum(site_weight))
    site_share = site_weight / weight_total
    log_b = jnp.log(site_share)
    shifted = EPSILON * jnp.log(growth) - EPSILON * first_lse
    shifted_lse, growth_total = over_cells((shifted[:, None] - distance) / EPSILON, jnp.sum(growth))
    log_a = jnp.log(growth / growth_total)
    cell_pot = EPSILON * log_a - EPSILON * first_lse
    site_pot = EPSILON * log_b - EPSILON * (shifted_lse - jnp.log(growth_total))
    for turn in range(1, ROUNDS):
        lse, _ = over_sites((site_pot[None, :] - distance) / EPSILON, 0.0)
        cell_pot = EPSILON * log_a - EPSILON * lse
        lse, _ = over_cells((cell_pot[:, None] - distance) / EPSILON, 0.0)
        site_pot = EPSILON * log_b - EPSILON * lse
    gene_sites = site_rows // gene_count
    split_at = lax.axis_index("gene_1") * 2 + lax.axis_index("gene_0")
    site_from = split_at * gene_sites
    part_distance = lax.dynamic_slice_in_dim(distance, site_from, gene_sites, 1)
    part_pot = lax.dynamic_slice_in_dim(site_pot, site_from, gene_sites, 0)
    coupling = jnp.exp((cell_pot[:, None] + part_pot[None, :] - part_distance) / EPSILON).astype(
        jnp.bfloat16
    )
    carried = lax.dot_general(
        coupling, projected, (((0,), (0,)), ((), ())), preferred_element_type=jnp.float32
    )
    piece = summed_on_arrival(carried, "cell", 0)
    piece_rows = piece.shape[0]
    piece_at = site_from + lax.axis_index("cell") * piece_rows
    share_part = lax.dynamic_slice_in_dim(site_share, piece_at, piece_rows, 0)
    scaled = piece / share_part[:, None]
    barycenter = gathered_rows(gathered_rows(scaled, PLANE), "gene_1")
    return (cell_pot, site_pot, barycenter)


def solution(mesh):
    torus = Mesh(
        mesh.devices.reshape(2, 2, mesh.shape["cell"], mesh.shape["site"]),
        ("gene_0", "gene_1", "cell", "site"),
    )
    return jax.shard_map(
        shards,
        mesh=torus,
        in_specs=(P("cell", GENE), P(GENE, None), P("site", None), P("cell"), P("site")),
        out_specs=(P("cell"), P("site"), P("site", None)),
        check_vma=False,
    )
```

```python
import jax
import jax.numpy as jnp
from jax import lax
from jax.sharding import Mesh
from jax.sharding import PartitionSpec as P

ROUNDS = 2
GENE = ("gene_0", "gene_1")
GENE_SITE = ("gene_0", "gene_1", "site")
PLANE = ("gene_0", "cell")


EPSILON = 0.02


def from_everyone(x, axis):
    length = lax.axis_size(axis)
    return lax.all_to_all(jnp.broadcast_to(x[None], (length, *x.shape)), axis, 0, 0, tiled=True)


def split_up(x, dim, length):
    shape = x.shape
    tiles = x.reshape(*shape[:dim], length, shape[dim] // length, *shape[dim + 1 :])
    return jnp.moveaxis(tiles, dim, 0)


def summed_on_arrival(x, axis, dim):
    length = lax.axis_size(axis)
    tiles = lax.all_to_all(split_up(x, dim, length), axis, 0, 0, tiled=True)
    return jnp.sum(tiles, axis=0)


def gathered_rows(x, axis):
    tiles = from_everyone(x, axis)
    return tiles.reshape(tiles.shape[0] * tiles.shape[1], *tiles.shape[2:])


def lse_with_total(local_peak, local_sum, partial, axis):
    width = local_peak.shape[0]
    local_lse = local_peak + jnp.log(local_sum)
    line = jnp.concatenate([local_lse, jnp.broadcast_to(partial, (128,))])
    both = from_everyone(line, axis)
    lses = both[:, :width]
    total = jnp.sum(both[:, width])
    peak = jnp.max(lses, axis=0)
    summed = jnp.sum(jnp.exp(lses - peak[None]), axis=0)
    return peak + jnp.log(summed), total


def over_sites(scores, partial):
    local_peak = jnp.max(scores, axis=1)
    local_sum = jnp.sum(jnp.exp(scores - local_peak[:, None]), axis=1)
    return lse_with_total(local_peak, local_sum, partial, "site")


def over_cells(scores, partial):
    local_peak = jnp.max(scores, axis=0)
    local_sum = jnp.sum(jnp.exp(scores - local_peak[None, :]), axis=0)
    return lse_with_total(local_peak, local_sum, partial, "cell")


def shards(expr, proj_weight, centroids, growth, site_weight):
    cell_rows = expr.shape[0]
    site_rows = centroids.shape[0]
    features = proj_weight.shape[1]
    gene_count = lax.axis_size(GENE)
    site_count = lax.axis_size("site")
    block_rows = cell_rows // (gene_count * site_count)
    partial = jnp.dot(expr, proj_weight, preferred_element_type=jnp.float32)
    grouped = partial.reshape(gene_count, site_count, block_rows, features)
    own_rows = lax.dynamic_index_in_dim(grouped, lax.axis_index("site"), 1, keepdims=False)
    own_rows = own_rows.reshape(gene_count * block_rows, features)
    row_share = summed_on_arrival(own_rows, GENE, 0)
    projected = gathered_rows(row_share.astype(jnp.bfloat16), GENE_SITE)
    proj_f = projected.astype(jnp.float32)
    cent_f = centroids.astype(jnp.float32)
    proj_norm = jnp.sum(proj_f * proj_f, axis=1) / features
    cent_norm = jnp.sum(cent_f * cent_f, axis=1) / features
    cross = lax.dot_general(
        projected, centroids, (((1,), (1,)), ((), ())), preferred_element_type=jnp.float32
    )
    distance = proj_norm[:, None] + cent_norm[None, :] - 2.0 * cross / features
    site_pot = jnp.zeros((site_rows,), jnp.float32)
    first_lse, weight_total = over_sites((site_pot[None, :] - distance) / EPSILON, jnp.sum(site_weight))
    site_share = site_weight / weight_total
    log_b = jnp.log(site_share)
    shifted = EPSILON * jnp.log(growth) - EPSILON * first_lse
    shifted_lse, growth_total = over_cells((shifted[:, None] - distance) / EPSILON, jnp.sum(growth))
    log_a = jnp.log(growth / growth_total)
    cell_pot = EPSILON * log_a - EPSILON * first_lse
    site_pot = EPSILON * log_b - EPSILON * (shifted_lse - jnp.log(growth_total))
    for turn in range(1, ROUNDS):
        lse, _ = over_sites((site_pot[None, :] - distance) / EPSILON, 0.0)
        cell_pot = EPSILON * log_a - EPSILON * lse
        lse, _ = over_cells((cell_pot[:, None] - distance) / EPSILON, 0.0)
        site_pot = EPSILON * log_b - EPSILON * lse
    gene_sites = site_rows // gene_count
    split_at = lax.axis_index("gene_1") * 2 + lax.axis_index("gene_0")
    site_from = split_at * gene_sites
    part_distance = lax.dynamic_slice_in_dim(distance, site_from, gene_sites, 1)
    part_pot = lax.dynamic_slice_in_dim(site_pot, site_from, gene_sites, 0)
    coupling = jnp.exp((cell_pot[:, None] + part_pot[None, :] - part_distance) / EPSILON).astype(
        jnp.bfloat16
    )
    carried = lax.dot_general(
        coupling, projected, (((0,), (0,)), ((), ())), preferred_element_type=jnp.float32
    )
    piece = summed_on_arrival(carried, "cell", 0)
    piece_rows = piece.shape[0]
    piece_at = site_from + lax.axis_index("cell") * piece_rows
    share_part = lax.dynamic_slice_in_dim(site_share, piece_at, piece_rows, 0)
    scaled = piece / share_part[:, None]
    barycenter = gathered_rows(gathered_rows(scaled.astype(jnp.bfloat16), PLANE), "gene_1")
    barycenter = barycenter.astype(jnp.float32)
    return (cell_pot, site_pot, barycenter)


def solution(mesh):
    torus = Mesh(
        mesh.devices.reshape(2, 2, mesh.shape["cell"], mesh.shape["site"]),
        ("gene_0", "gene_1", "cell", "site"),
    )
    return jax.shard_map(
        shards,
        mesh=torus,
        in_specs=(P("cell", GENE), P(GENE, None), P("site", None), P("cell"), P("site")),
        out_specs=(P("cell"), P("site"), P("site", None)),
        check_vma=False,
    )
```

```python
import jax
import jax.numpy as jnp
from jax import lax
from jax.sharding import Mesh
from jax.sharding import PartitionSpec as P

ROUNDS = 2
GENE = ("gene_0", "gene_1")
GENE_SITE = ("gene_0", "gene_1", "site")
PLANE = ("gene_0", "cell")


EPSILON = 0.02


def from_everyone(x, axis):
    length = lax.axis_size(axis)
    return lax.all_to_all(jnp.broadcast_to(x[None], (length, *x.shape)), axis, 0, 0, tiled=True)


def split_up(x, dim, length):
    shape = x.shape
    tiles = x.reshape(*shape[:dim], length, shape[dim] // length, *shape[dim + 1 :])
    return jnp.moveaxis(tiles, dim, 0)


def summed_on_arrival(x, axis, dim):
    length = lax.axis_size(axis)
    tiles = lax.all_to_all(split_up(x, dim, length), axis, 0, 0, tiled=True)
    return jnp.sum(tiles, axis=0)


def gathered_rows(x, axis):
    tiles = from_everyone(x, axis)
    return tiles.reshape(tiles.shape[0] * tiles.shape[1], *tiles.shape[2:])


def lse_with_total(local_peak, local_sum, partial, axis):
    width = local_peak.shape[0]
    local_lse = local_peak + jnp.log(local_sum)
    line = jnp.concatenate([local_lse, jnp.broadcast_to(partial, (128,))])
    both = from_everyone(line, axis)
    lses = both[:, :width]
    total = jnp.sum(both[:, width])
    peak = jnp.max(lses, axis=0)
    summed = jnp.sum(jnp.exp(lses - peak[None]), axis=0)
    return peak + jnp.log(summed), total


def over_sites(scores, partial):
    local_peak = jnp.max(scores, axis=1)
    local_sum = jnp.sum(jnp.exp(scores - local_peak[:, None]), axis=1)
    return lse_with_total(local_peak, local_sum, partial, "site")


def over_cells(scores, partial):
    local_peak = jnp.max(scores, axis=0)
    local_sum = jnp.sum(jnp.exp(scores - local_peak[None, :]), axis=0)
    return lse_with_total(local_peak, local_sum, partial, "cell")


def shards(expr, proj_weight, centroids, growth, site_weight):
    cell_rows = expr.shape[0]
    site_rows = centroids.shape[0]
    features = proj_weight.shape[1]
    gene_count = lax.axis_size(GENE)
    site_count = lax.axis_size("site")
    block_rows = cell_rows // (gene_count * site_count)
    site_at = lax.axis_index("site") * block_rows
    own_rows = jnp.concatenate(
        [
            jnp.dot(
                lax.dynamic_slice_in_dim(expr, g * site_count * block_rows + site_at, block_rows, 0),
                proj_weight,
                preferred_element_type=jnp.float32,
            )
            for g in range(gene_count)
        ]
    )
    row_share = summed_on_arrival(own_rows, GENE, 0)
    projected = gathered_rows(row_share.astype(jnp.bfloat16), GENE_SITE)
    proj_f = projected.astype(jnp.float32)
    cent_f = centroids.astype(jnp.float32)
    proj_norm = jnp.sum(proj_f * proj_f, axis=1) / features
    cent_norm = jnp.sum(cent_f * cent_f, axis=1) / features
    cross = lax.dot_general(
        projected, centroids, (((1,), (1,)), ((), ())), preferred_element_type=jnp.float32
    )
    distance = proj_norm[:, None] + cent_norm[None, :] - 2.0 * cross / features
    site_pot = jnp.zeros((site_rows,), jnp.float32)
    first_lse, weight_total = over_sites((site_pot[None, :] - distance) / EPSILON, jnp.sum(site_weight))
    site_share = site_weight / weight_total
    log_b = jnp.log(site_share)
    shifted = EPSILON * jnp.log(growth) - EPSILON * first_lse
    shifted_lse, growth_total = over_cells((shifted[:, None] - distance) / EPSILON, jnp.sum(growth))
    log_a = jnp.log(growth / growth_total)
    cell_pot = EPSILON * log_a - EPSILON * first_lse
    site_pot = EPSILON * log_b - EPSILON * (shifted_lse - jnp.log(growth_total))
    for turn in range(1, ROUNDS):
        lse, _ = over_sites((site_pot[None, :] - distance) / EPSILON, 0.0)
        cell_pot = EPSILON * log_a - EPSILON * lse
        lse, _ = over_cells((cell_pot[:, None] - distance) / EPSILON, 0.0)
        site_pot = EPSILON * log_b - EPSILON * lse
    gene_sites = site_rows // gene_count
    split_at = lax.axis_index("gene_1") * 2 + lax.axis_index("gene_0")
    site_from = split_at * gene_sites
    part_distance = lax.dynamic_slice_in_dim(distance, site_from, gene_sites, 1)
    part_pot = lax.dynamic_slice_in_dim(site_pot, site_from, gene_sites, 0)
    coupling = jnp.exp((cell_pot[:, None] + part_pot[None, :] - part_distance) / EPSILON).astype(
        jnp.bfloat16
    )
    carried = lax.dot_general(
        coupling, projected, (((0,), (0,)), ((), ())), preferred_element_type=jnp.float32
    )
    piece = summed_on_arrival(carried, "cell", 0)
    piece_rows = piece.shape[0]
    piece_at = site_from + lax.axis_index("cell") * piece_rows
    share_part = lax.dynamic_slice_in_dim(site_share, piece_at, piece_rows, 0)
    scaled = piece / share_part[:, None]
    barycenter = gathered_rows(gathered_rows(scaled.astype(jnp.bfloat16), PLANE), "gene_1")
    barycenter = barycenter.astype(jnp.float32)
    return (cell_pot, site_pot, barycenter)


def solution(mesh):
    torus = Mesh(
        mesh.devices.reshape(2, 2, mesh.shape["cell"], mesh.shape["site"]),
        ("gene_0", "gene_1", "cell", "site"),
    )
    return jax.shard_map(
        shards,
        mesh=torus,
        in_specs=(P("cell", GENE), P(GENE, None), P("site", None), P("cell"), P("site")),
        out_specs=(P("cell"), P("site"), P("site", None)),
        check_vma=False,
    )
```

```python
import jax
import jax.numpy as jnp
from jax import lax
from jax.sharding import Mesh
from jax.sharding import PartitionSpec as P

ROUNDS = 2
GENE = ("gene_0", "gene_1")
GENE_SITE = ("gene_0", "gene_1", "site")
PLANE = ("gene_0", "cell")
SITE_GENE = ("site", "gene_0", "gene_1")


EPSILON = 0.02


def from_everyone(x, axis):
    length = lax.axis_size(axis)
    return lax.all_to_all(jnp.broadcast_to(x[None], (length, *x.shape)), axis, 0, 0, tiled=True)


def split_up(x, dim, length):
    shape = x.shape
    tiles = x.reshape(*shape[:dim], length, shape[dim] // length, *shape[dim + 1 :])
    return jnp.moveaxis(tiles, dim, 0)


def summed_on_arrival(x, axis, dim):
    length = lax.axis_size(axis)
    tiles = lax.all_to_all(split_up(x, dim, length), axis, 0, 0, tiled=True)
    return jnp.sum(tiles, axis=0)


def gathered_rows(x, axis):
    tiles = from_everyone(x, axis)
    return tiles.reshape(tiles.shape[0] * tiles.shape[1], *tiles.shape[2:])


def lse_with_total(local_peak, local_sum, partial, axis):
    width = local_peak.shape[0]
    local_lse = local_peak + jnp.log(local_sum)
    line = jnp.concatenate([local_lse, jnp.broadcast_to(partial, (128,))])
    both = from_everyone(line, axis)
    lses = both[:, :width]
    total = jnp.sum(both[:, width])
    peak = jnp.max(lses, axis=0)
    summed = jnp.sum(jnp.exp(lses - peak[None]), axis=0)
    return peak + jnp.log(summed), total


def over_sites(scores, partial):
    local_peak = jnp.max(scores, axis=1)
    local_sum = jnp.sum(jnp.exp(scores - local_peak[:, None]), axis=1)
    return lse_with_total(local_peak, local_sum, partial, "site")


def over_cells(scores, partial):
    local_peak = jnp.max(scores, axis=0)
    local_sum = jnp.sum(jnp.exp(scores - local_peak[None, :]), axis=0)
    return lse_with_total(local_peak, local_sum, partial, "cell")


def shards(expr, proj_weight, centroids, growth, site_weight):
    cell_rows = expr.shape[0]
    site_rows = centroids.shape[0]
    features = proj_weight.shape[1]
    gene_count = lax.axis_size(GENE)
    site_count = lax.axis_size("site")
    block_rows = cell_rows // (gene_count * site_count)
    own_count = gene_count * block_rows
    own_block = lax.dynamic_slice_in_dim(expr, lax.axis_index("site") * own_count, own_count, 0)
    own_rows = jnp.dot(own_block, proj_weight, preferred_element_type=jnp.float32)
    row_share = summed_on_arrival(own_rows, GENE, 0)
    projected = gathered_rows(row_share.astype(jnp.bfloat16), SITE_GENE)
    proj_f = projected.astype(jnp.float32)
    cent_f = centroids.astype(jnp.float32)
    proj_norm = jnp.sum(proj_f * proj_f, axis=1) / features
    cent_norm = jnp.sum(cent_f * cent_f, axis=1) / features
    cross = lax.dot_general(
        projected, centroids, (((1,), (1,)), ((), ())), preferred_element_type=jnp.float32
    )
    distance = proj_norm[:, None] + cent_norm[None, :] - 2.0 * cross / features
    site_pot = jnp.zeros((site_rows,), jnp.float32)
    first_lse, weight_total = over_sites((site_pot[None, :] - distance) / EPSILON, jnp.sum(site_weight))
    site_share = site_weight / weight_total
    log_b = jnp.log(site_share)
    shifted = EPSILON * jnp.log(growth) - EPSILON * first_lse
    shifted_lse, growth_total = over_cells((shifted[:, None] - distance) / EPSILON, jnp.sum(growth))
    log_a = jnp.log(growth / growth_total)
    cell_pot = EPSILON * log_a - EPSILON * first_lse
    site_pot = EPSILON * log_b - EPSILON * (shifted_lse - jnp.log(growth_total))
    for turn in range(1, ROUNDS):
        lse, _ = over_sites((site_pot[None, :] - distance) / EPSILON, 0.0)
        cell_pot = EPSILON * log_a - EPSILON * lse
        lse, _ = over_cells((cell_pot[:, None] - distance) / EPSILON, 0.0)
        site_pot = EPSILON * log_b - EPSILON * lse
    gene_sites = site_rows // gene_count
    split_at = lax.axis_index("gene_1") * 2 + lax.axis_index("gene_0")
    site_from = split_at * gene_sites
    part_distance = lax.dynamic_slice_in_dim(distance, site_from, gene_sites, 1)
    part_pot = lax.dynamic_slice_in_dim(site_pot, site_from, gene_sites, 0)
    coupling = jnp.exp((cell_pot[:, None] + part_pot[None, :] - part_distance) / EPSILON).astype(
        jnp.bfloat16
    )
    carried = lax.dot_general(
        coupling, projected, (((0,), (0,)), ((), ())), preferred_element_type=jnp.float32
    )
    piece = summed_on_arrival(carried, "cell", 0)
    piece_rows = piece.shape[0]
    piece_at = site_from + lax.axis_index("cell") * piece_rows
    share_part = lax.dynamic_slice_in_dim(site_share, piece_at, piece_rows, 0)
    scaled = piece / share_part[:, None]
    barycenter = gathered_rows(gathered_rows(scaled.astype(jnp.bfloat16), PLANE), "gene_1")
    barycenter = barycenter.astype(jnp.float32)
    return (cell_pot, site_pot, barycenter)


def solution(mesh):
    torus = Mesh(
        mesh.devices.reshape(2, 2, mesh.shape["cell"], mesh.shape["site"]),
        ("gene_0", "gene_1", "cell", "site"),
    )
    return jax.shard_map(
        shards,
        mesh=torus,
        in_specs=(P("cell", GENE), P(GENE, None), P("site", None), P("cell"), P("site")),
        out_specs=(P("cell"), P("site"), P("site", None)),
        check_vma=False,
    )
```

```python
import jax
import jax.numpy as jnp
from jax import lax
from jax.sharding import Mesh
from jax.sharding import PartitionSpec as P

ROUNDS = 2
GENE = ("gene_0", "gene_1")
GENE_SITE = ("gene_0", "gene_1", "site")
SITE_GENE = ("site", "gene_0", "gene_1")


EPSILON = 0.02


def from_everyone(x, axis):
    length = lax.axis_size(axis)
    return lax.all_to_all(jnp.broadcast_to(x[None], (length, *x.shape)), axis, 0, 0, tiled=True)


def split_up(x, dim, length):
    shape = x.shape
    tiles = x.reshape(*shape[:dim], length, shape[dim] // length, *shape[dim + 1 :])
    return jnp.moveaxis(tiles, dim, 0)


def summed_on_arrival(x, axis, dim):
    length = lax.axis_size(axis)
    tiles = lax.all_to_all(split_up(x, dim, length), axis, 0, 0, tiled=True)
    return jnp.sum(tiles, axis=0)


def gathered_rows(x, axis):
    tiles = from_everyone(x, axis)
    return tiles.reshape(tiles.shape[0] * tiles.shape[1], *tiles.shape[2:])


def lse_with_total(local_peak, local_sum, partial, axis):
    width = local_peak.shape[0]
    local_lse = local_peak + jnp.log(local_sum)
    line = jnp.concatenate([local_lse, jnp.broadcast_to(partial, (128,))])
    both = from_everyone(line, axis)
    lses = both[:, :width]
    total = jnp.sum(both[:, width])
    peak = jnp.max(lses, axis=0)
    summed = jnp.sum(jnp.exp(lses - peak[None]), axis=0)
    return peak + jnp.log(summed), total


def over_sites(scores, partial):
    local_peak = jnp.max(scores, axis=1)
    local_sum = jnp.sum(jnp.exp(scores - local_peak[:, None]), axis=1)
    return lse_with_total(local_peak, local_sum, partial, "site")


def over_cells(scores, partial):
    local_peak = jnp.max(scores, axis=0)
    local_sum = jnp.sum(jnp.exp(scores - local_peak[None, :]), axis=0)
    return lse_with_total(local_peak, local_sum, partial, "cell")


def shards(expr, proj_weight, centroids, growth, site_weight):
    cell_rows = expr.shape[0]
    site_rows = centroids.shape[0]
    features = proj_weight.shape[1]
    gene_count = lax.axis_size(GENE)
    site_count = lax.axis_size("site")
    block_rows = cell_rows // (gene_count * site_count)
    own_count = gene_count * block_rows
    own_block = lax.dynamic_slice_in_dim(expr, lax.axis_index("site") * own_count, own_count, 0)
    own_rows = jnp.dot(own_block, proj_weight, preferred_element_type=jnp.float32)
    row_share = summed_on_arrival(own_rows, GENE, 0)
    projected = gathered_rows(row_share.astype(jnp.bfloat16), SITE_GENE)
    proj_f = projected.astype(jnp.float32)
    cent_f = centroids.astype(jnp.float32)
    proj_norm = jnp.sum(proj_f * proj_f, axis=1) / features
    cent_norm = jnp.sum(cent_f * cent_f, axis=1) / features
    cross = lax.dot_general(
        projected, centroids, (((1,), (1,)), ((), ())), preferred_element_type=jnp.float32
    )
    distance = proj_norm[:, None] + cent_norm[None, :] - 2.0 * cross / features
    site_pot = jnp.zeros((site_rows,), jnp.float32)
    first_lse, weight_total = over_sites((site_pot[None, :] - distance) / EPSILON, jnp.sum(site_weight))
    site_share = site_weight / weight_total
    log_b = jnp.log(site_share)
    shifted = EPSILON * jnp.log(growth) - EPSILON * first_lse
    shifted_lse, growth_total = over_cells((shifted[:, None] - distance) / EPSILON, jnp.sum(growth))
    log_a = jnp.log(growth / growth_total)
    cell_pot = EPSILON * log_a - EPSILON * first_lse
    site_pot = EPSILON * log_b - EPSILON * (shifted_lse - jnp.log(growth_total))
    for turn in range(1, ROUNDS):
        lse, _ = over_sites((site_pot[None, :] - distance) / EPSILON, 0.0)
        cell_pot = EPSILON * log_a - EPSILON * lse
        lse, _ = over_cells((cell_pot[:, None] - distance) / EPSILON, 0.0)
        site_pot = EPSILON * log_b - EPSILON * lse
    gene_sites = site_rows // gene_count
    split_at = lax.axis_index("gene_1") * 2 + lax.axis_index("gene_0")
    site_from = split_at * gene_sites
    part_distance = lax.dynamic_slice_in_dim(distance, site_from, gene_sites, 1)
    part_pot = lax.dynamic_slice_in_dim(site_pot, site_from, gene_sites, 0)
    coupling = jnp.exp((cell_pot[:, None] + part_pot[None, :] - part_distance) / EPSILON).astype(
        jnp.bfloat16
    )
    carried = lax.dot_general(
        coupling, projected, (((0,), (0,)), ((), ())), preferred_element_type=jnp.float32
    )
    piece = summed_on_arrival(carried, "cell", 0)
    piece_rows = piece.shape[0]
    piece_at = site_from + lax.axis_index("cell") * piece_rows
    share_part = lax.dynamic_slice_in_dim(site_share, piece_at, piece_rows, 0)
    scaled = piece / share_part[:, None]
    barycenter = gathered_rows(gathered_rows(scaled.astype(jnp.bfloat16), "cell"), "gene_0")
    barycenter = gathered_rows(barycenter, "gene_1")
    barycenter = barycenter.astype(jnp.float32)
    return (cell_pot, site_pot, barycenter)


def solution(mesh):
    torus = Mesh(
        mesh.devices.reshape(2, 2, mesh.shape["cell"], mesh.shape["site"]),
        ("gene_0", "gene_1", "cell", "site"),
    )
    return jax.shard_map(
        shards,
        mesh=torus,
        in_specs=(P("cell", GENE), P(GENE, None), P("site", None), P("cell"), P("site")),
        out_specs=(P("cell"), P("site"), P("site", None)),
        check_vma=False,
    )
```

```python
import jax
import jax.numpy as jnp
from jax import lax
from jax.experimental import pallas as pl
from jax.experimental.pallas import tpu as pltpu
from jax.sharding import Mesh
from jax.sharding import PartitionSpec as P

ROUNDS = 2
GENE = ("gene_0", "gene_1")
GENE_SITE = ("gene_0", "gene_1", "site")
PLANE = ("gene_0", "cell")
SITE_GENE = ("site", "gene_0", "gene_1")


EPSILON = 0.02


def from_everyone(x, axis):
    length = lax.axis_size(axis)
    return lax.all_to_all(jnp.broadcast_to(x[None], (length, *x.shape)), axis, 0, 0, tiled=True)


def split_up(x, dim, length):
    shape = x.shape
    tiles = x.reshape(*shape[:dim], length, shape[dim] // length, *shape[dim + 1 :])
    return jnp.moveaxis(tiles, dim, 0)


def summed_on_arrival(x, axis, dim):
    length = lax.axis_size(axis)
    tiles = lax.all_to_all(split_up(x, dim, length), axis, 0, 0, tiled=True)
    return jnp.sum(tiles, axis=0)


def gathered_rows(x, axis):
    tiles = from_everyone(x, axis)
    return tiles.reshape(tiles.shape[0] * tiles.shape[1], *tiles.shape[2:])


def lse_with_total(local_lse, partial, axis):
    width = local_lse.shape[0]
    line = jnp.concatenate([local_lse, jnp.broadcast_to(partial, (128,))])
    both = from_everyone(line, axis)
    lses = both[:, :width]
    total = jnp.sum(both[:, width])
    peak = jnp.max(lses, axis=0)
    summed = jnp.sum(jnp.exp(lses - peak[None]), axis=0)
    return peak + jnp.log(summed), total


def row_lse_kernel(pot_ref, d_ref, out_ref):
    scores = (pot_ref[...] - d_ref[...]) / EPSILON
    peak = jnp.max(scores, axis=1, keepdims=True)
    summed = jnp.sum(jnp.exp(scores - peak), axis=1, keepdims=True)
    out_ref[...] = peak + jnp.log(summed)


def col_lse_kernel(pot_ref, d_ref, out_ref):
    scores = (pot_ref[...] - d_ref[...]) / EPSILON
    peak = jnp.max(scores, axis=0, keepdims=True)
    summed = jnp.sum(jnp.exp(scores - peak), axis=0, keepdims=True)
    out_ref[...] = peak + jnp.log(summed)


def over_sites(site_pot, distance, partial):
    rows, cols = distance.shape
    tile = 128
    local_lse = pl.pallas_call(
        row_lse_kernel,
        grid=(rows // tile,),
        in_specs=[
            pl.BlockSpec((1, cols), lambda i: (0, 0)),
            pl.BlockSpec((tile, cols), lambda i: (i, 0)),
        ],
        out_specs=pl.BlockSpec((tile, 1), lambda i: (i, 0)),
        out_shape=jax.ShapeDtypeStruct((rows, 1), jnp.float32),
        cost_estimate=pl.CostEstimate(
            flops=4 * rows * cols, transcendentals=rows * cols, bytes_accessed=4 * rows * cols
        ),
    )(site_pot[None, :], distance)
    return lse_with_total(local_lse[:, 0], partial, "site")


def over_cells(cell_pot, distance, partial):
    rows, cols = distance.shape
    tile = 512
    local_lse = pl.pallas_call(
        col_lse_kernel,
        grid=(cols // tile,),
        in_specs=[
            pl.BlockSpec((rows, 1), lambda j: (0, 0)),
            pl.BlockSpec((rows, tile), lambda j: (0, j)),
        ],
        out_specs=pl.BlockSpec((1, tile), lambda j: (0, j)),
        out_shape=jax.ShapeDtypeStruct((1, cols), jnp.float32),
        cost_estimate=pl.CostEstimate(
            flops=4 * rows * cols, transcendentals=rows * cols, bytes_accessed=4 * rows * cols
        ),
    )(cell_pot[:, None], distance)
    return lse_with_total(local_lse[0], partial, "cell")


def shards(expr, proj_weight, centroids, growth, site_weight):
    cell_rows = expr.shape[0]
    site_rows = centroids.shape[0]
    features = proj_weight.shape[1]
    gene_count = lax.axis_size(GENE)
    site_count = lax.axis_size("site")
    block_rows = cell_rows // (gene_count * site_count)
    own_count = gene_count * block_rows
    own_block = lax.dynamic_slice_in_dim(expr, lax.axis_index("site") * own_count, own_count, 0)
    own_rows = jnp.dot(own_block, proj_weight, preferred_element_type=jnp.float32)
    row_share = summed_on_arrival(own_rows, GENE, 0)
    projected = gathered_rows(row_share.astype(jnp.bfloat16), SITE_GENE)
    proj_f = projected.astype(jnp.float32)
    cent_f = centroids.astype(jnp.float32)
    proj_norm = jnp.sum(proj_f * proj_f, axis=1) / features
    cent_norm = jnp.sum(cent_f * cent_f, axis=1) / features
    cross = lax.dot_general(
        projected, centroids, (((1,), (1,)), ((), ())), preferred_element_type=jnp.float32
    )
    distance = proj_norm[:, None] + cent_norm[None, :] - 2.0 * cross / features
    site_pot = jnp.zeros((site_rows,), jnp.float32)
    first_lse, weight_total = over_sites(site_pot, distance, jnp.sum(site_weight))
    site_share = site_weight / weight_total
    log_b = jnp.log(site_share)
    shifted = EPSILON * jnp.log(growth) - EPSILON * first_lse
    shifted_lse, growth_total = over_cells(shifted, distance, jnp.sum(growth))
    log_a = jnp.log(growth / growth_total)
    cell_pot = EPSILON * log_a - EPSILON * first_lse
    site_pot = EPSILON * log_b - EPSILON * (shifted_lse - jnp.log(growth_total))
    for turn in range(1, ROUNDS):
        lse, _ = over_sites(site_pot, distance, 0.0)
        cell_pot = EPSILON * log_a - EPSILON * lse
        lse, _ = over_cells(cell_pot, distance, 0.0)
        site_pot = EPSILON * log_b - EPSILON * lse
    gene_sites = site_rows // gene_count
    split_at = lax.axis_index("gene_1") * 2 + lax.axis_index("gene_0")
    site_from = split_at * gene_sites
    part_distance = lax.dynamic_slice_in_dim(distance, site_from, gene_sites, 1)
    part_pot = lax.dynamic_slice_in_dim(site_pot, site_from, gene_sites, 0)
    coupling = jnp.exp((cell_pot[:, None] + part_pot[None, :] - part_distance) / EPSILON).astype(
        jnp.bfloat16
    )
    carried = lax.dot_general(
        coupling, projected, (((0,), (0,)), ((), ())), preferred_element_type=jnp.float32
    )
    piece = summed_on_arrival(carried, "cell", 0)
    piece_rows = piece.shape[0]
    piece_at = site_from + lax.axis_index("cell") * piece_rows
    share_part = lax.dynamic_slice_in_dim(site_share, piece_at, piece_rows, 0)
    scaled = piece / share_part[:, None]
    barycenter = gathered_rows(gathered_rows(scaled.astype(jnp.bfloat16), PLANE), "gene_1")
    barycenter = barycenter.astype(jnp.float32)
    return (cell_pot, site_pot, barycenter)


def solution(mesh):
    torus = Mesh(
        mesh.devices.reshape(2, 2, mesh.shape["cell"], mesh.shape["site"]),
        ("gene_0", "gene_1", "cell", "site"),
    )
    return jax.shard_map(
        shards,
        mesh=torus,
        in_specs=(P("cell", GENE), P(GENE, None), P("site", None), P("cell"), P("site")),
        out_specs=(P("cell"), P("site"), P("site", None)),
        check_vma=False,
    )
```

```python
import jax
import jax.numpy as jnp
from jax import lax
from jax.sharding import Mesh
from jax.sharding import PartitionSpec as P

ROUNDS = 2
GENE = ("gene_0", "gene_1")
GENE_SITE = ("gene_0", "gene_1", "site")
PLANE = ("gene_0", "cell")
SITE_GENE = ("site", "gene_0", "gene_1")


EPSILON = 0.02


def from_everyone(x, axis):
    length = lax.axis_size(axis)
    return lax.all_to_all(jnp.broadcast_to(x[None], (length, *x.shape)), axis, 0, 0, tiled=True)


def split_up(x, dim, length):
    shape = x.shape
    tiles = x.reshape(*shape[:dim], length, shape[dim] // length, *shape[dim + 1 :])
    return jnp.moveaxis(tiles, dim, 0)


def summed_on_arrival(x, axis, dim):
    length = lax.axis_size(axis)
    tiles = lax.all_to_all(split_up(x, dim, length), axis, 0, 0, tiled=True)
    return jnp.sum(tiles, axis=0)


def gathered_rows(x, axis):
    tiles = from_everyone(x, axis)
    return tiles.reshape(tiles.shape[0] * tiles.shape[1], *tiles.shape[2:])


def lse_with_total(local_peak, local_sum, partial, axis):
    width = local_peak.shape[0]
    local_lse = local_peak + jnp.log(local_sum)
    line = jnp.concatenate([local_lse, jnp.broadcast_to(partial, (128,))])
    both = from_everyone(line, axis)
    lses = both[:, :width]
    total = jnp.sum(both[:, width])
    peak = jnp.max(lses, axis=0)
    summed = jnp.sum(jnp.exp(lses - peak[None]), axis=0)
    return peak + jnp.log(summed), total


def over_sites(scores, partial):
    local_peak = jnp.max(scores, axis=1)
    local_sum = jnp.sum(jnp.exp(scores - local_peak[:, None]), axis=1)
    return lse_with_total(local_peak, local_sum, partial, "site")


def over_cells(scores, partial):
    local_peak = jnp.max(scores, axis=0)
    local_sum = jnp.sum(jnp.exp(scores - local_peak[None, :]), axis=0)
    return lse_with_total(local_peak, local_sum, partial, "cell")


def shards(expr, proj_weight, centroids, growth, site_weight):
    cell_rows = expr.shape[0]
    site_rows = centroids.shape[0]
    features = proj_weight.shape[1]
    gene_count = lax.axis_size(GENE)
    site_count = lax.axis_size("site")
    block_rows = cell_rows // (gene_count * site_count)
    own_count = gene_count * block_rows
    own_block = lax.dynamic_slice_in_dim(expr, lax.axis_index("site") * own_count, own_count, 0)
    own_rows = jnp.dot(own_block, proj_weight, preferred_element_type=jnp.float32)
    row_share = summed_on_arrival(own_rows, GENE, 0)
    projected = gathered_rows(row_share.astype(jnp.bfloat16), SITE_GENE)
    proj_f = projected.astype(jnp.float32)
    cent_f = centroids.astype(jnp.float32)
    proj_norm = jnp.sum(proj_f * proj_f, axis=1) / features
    cent_norm = jnp.sum(cent_f * cent_f, axis=1) / features
    cross = lax.dot_general(
        projected, centroids, (((1,), (1,)), ((), ())), preferred_element_type=jnp.float32
    )
    distance = proj_norm[:, None] + cent_norm[None, :] - 2.0 * cross / features
    site_pot = jnp.zeros((site_rows,), jnp.float32)
    first_lse, weight_total = over_sites((site_pot[None, :] - distance) / EPSILON, jnp.sum(site_weight))
    site_share = site_weight / weight_total
    log_b = jnp.log(site_share)
    shifted = EPSILON * jnp.log(growth) - EPSILON * first_lse
    shifted_lse, growth_total = over_cells((shifted[:, None] - distance) / EPSILON, jnp.sum(growth))
    log_a = jnp.log(growth / growth_total)
    cell_pot = EPSILON * log_a - EPSILON * first_lse
    site_pot = EPSILON * log_b - EPSILON * (shifted_lse - jnp.log(growth_total))
    for turn in range(1, ROUNDS - 1):
        lse, _ = over_sites((site_pot[None, :] - distance) / EPSILON, 0.0)
        cell_pot = EPSILON * log_a - EPSILON * lse
        lse, _ = over_cells((cell_pot[:, None] - distance) / EPSILON, 0.0)
        site_pot = EPSILON * log_b - EPSILON * lse
    lse, _ = over_sites((site_pot[None, :] - distance) / EPSILON, 0.0)
    cell_pot = EPSILON * log_a - EPSILON * lse
    scores = (cell_pot[:, None] - distance) / EPSILON
    local_peak = jnp.max(scores, axis=0)
    local_lse = local_peak + jnp.log(jnp.sum(jnp.exp(scores - local_peak[None, :]), axis=0))
    gene_sites = site_rows // gene_count
    split_at = lax.axis_index("gene_1") * 2 + lax.axis_index("gene_0")
    site_from = split_at * gene_sites
    part_scores = lax.dynamic_slice_in_dim(scores, site_from, gene_sites, 1)
    part_lse = lax.dynamic_slice_in_dim(local_lse, site_from, gene_sites, 0)
    weights = jnp.exp(part_scores - part_lse[None, :])
    carried = lax.dot_general(
        weights,
        proj_f,
        (((0,), (0,)), ((), ())),
        precision=lax.Precision.HIGHEST,
        preferred_element_type=jnp.float32,
    )
    cell_count = lax.axis_size("cell")
    piece_rows = gene_sites // cell_count
    tile_size = piece_rows * features
    lines = jnp.concatenate(
        [
            carried.reshape(cell_count, tile_size),
            jnp.broadcast_to(local_lse[None], (cell_count, site_rows)),
        ],
        axis=1,
    )
    arrived = lax.all_to_all(lines, "cell", 0, 0, tiled=True)
    got_tiles = arrived[:, :tile_size].reshape(cell_count, piece_rows, features)
    got_lse = arrived[:, tile_size:]
    peak = jnp.max(got_lse, axis=0)
    total_lse = peak + jnp.log(jnp.sum(jnp.exp(got_lse - peak[None]), axis=0))
    site_pot = EPSILON * log_b - EPSILON * total_lse
    piece_at = site_from + lax.axis_index("cell") * piece_rows
    mine = lax.dynamic_slice_in_dim(got_lse, piece_at, piece_rows, 1)
    mine_total = lax.dynamic_slice_in_dim(total_lse, piece_at, piece_rows, 0)
    mine_log_b = lax.dynamic_slice_in_dim(log_b, piece_at, piece_rows, 0)
    factor = jnp.exp(mine_log_b[None, :] + mine - mine_total[None, :])
    piece = jnp.sum(factor[:, :, None] * got_tiles, axis=0)
    share_part = lax.dynamic_slice_in_dim(site_share, piece_at, piece_rows, 0)
    scaled = piece / share_part[:, None]
    barycenter = gathered_rows(gathered_rows(scaled.astype(jnp.bfloat16), PLANE), "gene_1")
    barycenter = barycenter.astype(jnp.float32)
    return (cell_pot, site_pot, barycenter)


def solution(mesh):
    torus = Mesh(
        mesh.devices.reshape(2, 2, mesh.shape["cell"], mesh.shape["site"]),
        ("gene_0", "gene_1", "cell", "site"),
    )
    return jax.shard_map(
        shards,
        mesh=torus,
        in_specs=(P("cell", GENE), P(GENE, None), P("site", None), P("cell"), P("site")),
        out_specs=(P("cell"), P("site"), P("site", None)),
        check_vma=False,
    )
```

```python
import jax
import jax.numpy as jnp
from jax import lax
from jax.sharding import Mesh
from jax.sharding import PartitionSpec as P

ROUNDS = 2
GENE = ("gene_0", "gene_1")
GENE_SITE = ("gene_0", "gene_1", "site")
PLANE = ("gene_0", "cell")
SITE_GENE = ("site", "gene_0", "gene_1")


EPSILON = 0.02


def from_everyone(x, axis):
    length = lax.axis_size(axis)
    return lax.all_to_all(jnp.broadcast_to(x[None], (length, *x.shape)), axis, 0, 0, tiled=True)


def split_up(x, dim, length):
    shape = x.shape
    tiles = x.reshape(*shape[:dim], length, shape[dim] // length, *shape[dim + 1 :])
    return jnp.moveaxis(tiles, dim, 0)


def summed_on_arrival(x, axis, dim):
    length = lax.axis_size(axis)
    tiles = lax.all_to_all(split_up(x, dim, length), axis, 0, 0, tiled=True)
    return jnp.sum(tiles, axis=0)


def gathered_rows(x, axis):
    tiles = from_everyone(x, axis)
    return tiles.reshape(tiles.shape[0] * tiles.shape[1], *tiles.shape[2:])


def lse_with_total(local_peak, local_sum, partial, axis):
    width = local_peak.shape[0]
    local_lse = local_peak + jnp.log(local_sum)
    line = jnp.concatenate([local_lse, jnp.broadcast_to(partial, (128,))])
    both = from_everyone(line, axis)
    lses = both[:, :width]
    total = jnp.sum(both[:, width])
    peak = jnp.max(lses, axis=0)
    summed = jnp.sum(jnp.exp(lses - peak[None]), axis=0)
    return peak + jnp.log(summed), total


def over_sites(scores, partial):
    local_peak = jnp.max(scores, axis=1)
    local_sum = jnp.sum(jnp.exp(scores - local_peak[:, None]), axis=1)
    return lse_with_total(local_peak, local_sum, partial, "site")


def over_cells(scores, partial):
    local_peak = jnp.max(scores, axis=0)
    local_sum = jnp.sum(jnp.exp(scores - local_peak[None, :]), axis=0)
    return lse_with_total(local_peak, local_sum, partial, "cell")


def shards(expr, proj_weight, centroids, growth, site_weight):
    cell_rows = expr.shape[0]
    site_rows = centroids.shape[0]
    features = proj_weight.shape[1]
    gene_count = lax.axis_size(GENE)
    site_count = lax.axis_size("site")
    block_rows = cell_rows // (gene_count * site_count)
    own_count = gene_count * block_rows
    own_block = lax.dynamic_slice_in_dim(expr, lax.axis_index("site") * own_count, own_count, 0)
    own_rows = jnp.dot(own_block, proj_weight, preferred_element_type=jnp.float32)
    row_share = summed_on_arrival(own_rows, GENE, 0)
    projected = gathered_rows(row_share.astype(jnp.bfloat16), SITE_GENE)
    proj_f = projected.astype(jnp.float32)
    cent_f = centroids.astype(jnp.float32)
    proj_norm = jnp.sum(proj_f * proj_f, axis=1) / features
    cent_norm = jnp.sum(cent_f * cent_f, axis=1) / features
    cross = lax.dot_general(
        projected, centroids, (((1,), (1,)), ((), ())), preferred_element_type=jnp.float32
    )
    distance = proj_norm[:, None] + cent_norm[None, :] - 2.0 * cross / features
    site_pot = jnp.zeros((site_rows,), jnp.float32)
    first_lse, weight_total = over_sites((site_pot[None, :] - distance) / EPSILON, jnp.sum(site_weight))
    site_share = site_weight / weight_total
    log_b = jnp.log(site_share)
    shifted = EPSILON * jnp.log(growth) - EPSILON * first_lse
    shifted_lse, growth_total = over_cells((shifted[:, None] - distance) / EPSILON, jnp.sum(growth))
    log_a = jnp.log(growth / growth_total)
    cell_pot = EPSILON * log_a - EPSILON * first_lse
    site_pot = EPSILON * log_b - EPSILON * (shifted_lse - jnp.log(growth_total))
    for turn in range(1, ROUNDS):
        fresh, site_pot = lax.optimization_barrier((projected, site_pot))
        cross = lax.dot_general(
            fresh, centroids, (((1,), (1,)), ((), ())), preferred_element_type=jnp.float32
        )
        distance = proj_norm[:, None] + cent_norm[None, :] - 2.0 * cross / features
        lse, _ = over_sites((site_pot[None, :] - distance) / EPSILON, 0.0)
        cell_pot = EPSILON * log_a - EPSILON * lse
        lse, _ = over_cells((cell_pot[:, None] - distance) / EPSILON, 0.0)
        site_pot = EPSILON * log_b - EPSILON * lse
    gene_sites = site_rows // gene_count
    split_at = lax.axis_index("gene_1") * 2 + lax.axis_index("gene_0")
    site_from = split_at * gene_sites
    part_distance = lax.dynamic_slice_in_dim(distance, site_from, gene_sites, 1)
    part_pot = lax.dynamic_slice_in_dim(site_pot, site_from, gene_sites, 0)
    coupling = jnp.exp((cell_pot[:, None] + part_pot[None, :] - part_distance) / EPSILON).astype(
        jnp.bfloat16
    )
    carried = lax.dot_general(
        coupling, projected, (((0,), (0,)), ((), ())), preferred_element_type=jnp.float32
    )
    piece = summed_on_arrival(carried, "cell", 0)
    piece_rows = piece.shape[0]
    piece_at = site_from + lax.axis_index("cell") * piece_rows
    share_part = lax.dynamic_slice_in_dim(site_share, piece_at, piece_rows, 0)
    scaled = piece / share_part[:, None]
    barycenter = gathered_rows(gathered_rows(scaled.astype(jnp.bfloat16), PLANE), "gene_1")
    barycenter = barycenter.astype(jnp.float32)
    return (cell_pot, site_pot, barycenter)


def solution(mesh):
    torus = Mesh(
        mesh.devices.reshape(2, 2, mesh.shape["cell"], mesh.shape["site"]),
        ("gene_0", "gene_1", "cell", "site"),
    )
    return jax.shard_map(
        shards,
        mesh=torus,
        in_specs=(P("cell", GENE), P(GENE, None), P("site", None), P("cell"), P("site")),
        out_specs=(P("cell"), P("site"), P("site", None)),
        check_vma=False,
    )
```
